128 devices in a mesh: expert: 32 (over x, y, core), hidden: 4 (over z).
Axes of the slice: x: 4, y: 4, z: 4, core: 2. Of those that a mesh axis runs over, the one named last changes fastest.
Arguments:
- tokens: bfloat16 [4096, 4096], P('expert', 'hidden'), may hold values from -6 to 6
- w_gate: bfloat16 [64, 4096, 1536], P('expert', None, 'hidden'), may hold values from -0.09375 to 0.09375
- w_up: bfloat16 [64, 4096, 1536], P('expert', None, 'hidden'), may hold values from -0.09375 to 0.09375
- w_down: bfloat16 [64, 1536, 4096], P('expert', 'hidden'), may hold values from -0.15625 to 0.15625
- routes: int32 [4096, 8], P('expert'), may hold values from 0 to 63, all different within a row; in each aligned block of 128 rows (0 to 127, 128 to 255, ...) at most 24 rows name the same one
- gate_levels: int32 [4096, 8], P('expert'), may hold values from 1 to 16
- ancestors: int32 [4096], P('expert'), may hold values from 0 to 127
Outputs:
- mixed: bfloat16 [4096, 4096], P('expert', 'hidden')
The draws below stay inside these ranges and needn't reach their ends.
Inputs may be any that keep to these rules, and one draw needn't show every extreme that they name: `routes`: in each aligned block of 128 rows no expert is chosen by more than 24 rows, a bound that some block reaches; a row chooses 8 different experts. `ancestors`: an ancestor lies in the same aligned block of 128 rows.
All inputs are finite; a program needn't handle non-finite values.
Results may differ from the reference program's by a relative error of at most 0.014.
Values may be sent and summed in bfloat16 or wider, within the bound.
No kernel may reach another device: no remote copies, remote signals or barrier semaphores. Data moves between devices by JAX's collectives and lax.ppermute only.
A program may use at most 192 MiB of HBM per device.

```python
import math
import jax
import jax.numpy as jnp
import numpy as np
from jax import lax

D = 4096
FF = 1536
TOP = 8
ROW_DEV = 128
EXPERTS = 64
ROWS = 4096
CAP = 24
N_EXPERT = 32


def place_ends(values, key, smallest, top_value):
    longest = values.shape.index(max(values.shape))
    spots = []
    for shift in (0, 1):
        where = [jax.random.randint(jax.random.fold_in(key, axis), (), 0, length) for axis, length in enumerate(values.shape)]
        where[longest] = (where[longest] + shift) % values.shape[longest]
        spots.append(tuple(where))
    return values.at[spots[0]].set(smallest).at[spots[1]].set(top_value)


def steps_of(rng, dims, cuts, low, largest):
    loudness = 1.0
    for axis_at, blocks in cuts:
        draws = jax.random.uniform(jax.random.fold_in(jax.random.fold_in(rng, 6), axis_at), (blocks,), jnp.float32, low / len(cuts), largest / len(cuts))
        loudness = loudness * jnp.repeat(jnp.exp(draws), dims[axis_at] // blocks).reshape((-1,) + (1,) * (len(dims) - 1 - axis_at))
    return loudness


def shared_out(own_key, own, number, rows, count, top, limit, lean):
    ranking = jax.random.permutation(own_key, count)
    crowded, usual = portions_of(count, rows * top, limit, lean, True), portions_of(count, rows * top, limit, lean, False)
    places = jnp.arange(count)

    def named(lengths, rotation):
        used = int((lengths > 0).sum())
        fixed = max(1, used // 4)
        shifted = fixed + (places - fixed + rotation * (used - fixed)) % max(1, count - fixed)
        return jnp.zeros((count,), jnp.int32).at[ranking[jnp.where(places < fixed, places, shifted)]].set(jnp.asarray(lengths, jnp.int32))

    lengths = jnp.where(number % 4 == 0, named(crowded, number // 4), named(usual, number - number // 4 - 1))
    mixed = jax.random.permutation(jax.random.fold_in(own, 3), count)
    donor, taker = mixed[0:count // 2 * 2:2], mixed[1:count // 2 * 2:2]
    margin = jnp.minimum(lengths[donor] - 1, limit - lengths[taker]) // 2
    margin = jnp.where((donor == ranking[0]) | (taker == ranking[0]) | (lengths[taker] == 0), 0, jnp.maximum(margin, 0))
    shifted = jax.random.randint(jax.random.fold_in(own, 4), (count // 2,), 0, 1 << 20) % (margin + 1)
    lengths = lengths.at[donor].add(-shifted).at[taker].add(shifted)
    items = jnp.searchsorted(jnp.cumsum(lengths), jnp.arange(rows * top), side="right").astype(jnp.int32)
    grid = items.reshape(top, rows).T
    grid = grid[jax.random.permutation(jax.random.fold_in(own, 1), rows)]
    rotation = jax.random.randint(jax.random.fold_in(own, 2), (rows, 1), 0, top)
    return jnp.take_along_axis(grid, (jnp.arange(top)[None, :] + rotation) % top, axis=1)


def portions_of(count, total, limit, lean, full):
    portions = [(1 << 20) // math.isqrt(grade ** lean) + 1 for grade in range(1, count + 1)]
    largest = limit if full else min(limit, max(-(-total // count), total * portions[0] // sum(portions)))
    least = 1 if total - largest >= count - 1 else 0
    given, surplus = [largest] + [least] * (count - 1), total - largest - least * (count - 1)
    while surplus > 0:
        candidates = [i for i in range(1, count) if given[i] < largest] or [i for i in range(1, count) if given[i] < limit]
        mass, budget = sum([portions[i] for i in candidates]), surplus
        for i in candidates:
            addition = min(limit - given[i], max(1, budget * portions[i] // mass), surplus)
            given[i] = given[i] + addition
            surplus = surplus - addition
    return np.array(given)


def bell_draw(stream_key, extent, deviation, most, cuts=(), kind=jnp.bfloat16):
    values = jax.random.normal(stream_key, extent, jnp.float32) * deviation
    if len(cuts) > 0:
        values = steps_of(stream_key, extent, cuts, -0.22, 0.18) * values
    return jnp.clip(values, min=-most, max=most).astype(kind)


def setup_inputs(seed: int = 0) -> dict:
    key_of = jax.random.split(jax.random.key(seed), 8)
    tokens = bell_draw(key_of[0], (ROWS, D), 1.0, 6.0, ((0, 32), (1, 4)))
    w_gate = bell_draw(key_of[1], (EXPERTS, D, FF), D ** -0.5, 0.09375, ((0, 32), (2, 4)))
    w_up = bell_draw(key_of[2], (EXPERTS, D, FF), D ** -0.5, 0.09375, ((0, 32), (2, 4)))
    w_down = bell_draw(key_of[3], (EXPERTS, FF, D), FF ** -0.5, 0.15625, ((0, 32), (1, 4)))
    routes_keys = jax.random.split(jax.random.fold_in(key_of[4], 1), ROWS // ROW_DEV)
    routes_turns = jax.random.permutation(jax.random.fold_in(key_of[4], 3), ROWS // ROW_DEV)
    routes = jax.vmap(lambda own, number: shared_out(jax.random.fold_in(key_of[4], 2), own, number, ROW_DEV, EXPERTS, TOP, CAP, 2))(routes_keys, routes_turns).reshape((ROWS, TOP))
    gate_levels = place_ends(jax.random.randint(key_of[5], (ROWS, TOP), 1, 17), jax.random.fold_in(key_of[5], 1), 1, 16).astype(jnp.int32)
    ancestors = place_ends(jax.random.randint(key_of[6], (ROWS,), 0, ROW_DEV), jax.random.fold_in(key_of[6], 1), 0, ROW_DEV - 1).astype(jnp.int32)
    return dict(tokens=tokens, w_gate=w_gate, w_up=w_up, w_down=w_down, routes=routes, gate_levels=gate_levels, ancestors=ancestors)


def reference(tokens, w_gate, w_up, w_down, routes, gate_levels, ancestors):
    rows_all = tokens.shape[0]
    choose = routes.shape[1]
    experts = w_gate.shape[0]
    width = tokens.shape[1]
    chosen = routes.reshape(-1).astype(jnp.int32)
    one_hot = (chosen[:, None] == jnp.arange(experts, dtype=jnp.int32)[None, :]).astype(jnp.int32)
    earlier = jnp.cumsum(one_hot, 0) - one_hot
    places = jnp.sum(earlier * one_hot, 1).astype(jnp.int32)
    bound = N_EXPERT * CAP
    target = (chosen * bound + places).astype(jnp.int32)
    row_ids = (jnp.arange(rows_all * choose, dtype=jnp.int32) // choose + 1).astype(jnp.int32)
    slot_rows = jnp.zeros((experts * bound,), jnp.int32).at[target].set(row_ids)
    padded = jnp.concatenate([jnp.zeros((1, width), tokens.dtype), tokens], 0)

    def expert_out(items):
        index_rows, gate_mat, up_mat, down_mat = items
        inputs = padded[index_rows].astype(jnp.float32)
        gate_acts = jnp.dot(inputs, gate_mat.astype(jnp.float32), precision=lax.Precision.HIGHEST)
        up_acts = jnp.dot(inputs, up_mat.astype(jnp.float32), precision=lax.Precision.HIGHEST)
        rounded = (jax.nn.silu(gate_acts) * up_acts).astype(jnp.bfloat16)
        rounded = lax.optimization_barrier(rounded)
        result = jnp.dot(rounded.astype(jnp.float32), down_mat.astype(jnp.float32), precision=lax.Precision.HIGHEST)
        return result.astype(jnp.bfloat16)

    outputs = lax.map(expert_out, (slot_rows.reshape(experts, bound), w_gate, w_up, w_down))
    picked = outputs.reshape(experts * bound, width)[target].astype(jnp.float32).reshape(rows_all, choose, width)
    levels = gate_levels.astype(jnp.float32)
    weights = levels / jnp.sum(levels, 1, keepdims=True)
    combined = jnp.sum(weights[:, :, None] * picked, 1)
    source = ((jnp.arange(rows_all, dtype=jnp.int32) // ROW_DEV) * ROW_DEV + ancestors).astype(jnp.int32)
    return combined[source].astype(jnp.bfloat16)
```

```python
import jax
import jax.numpy as jnp
from jax import lax
from jax.sharding import PartitionSpec as P

SPLIT = 2


def expert_chunk(send, w_gate, w_up, w_down):
    arrived = lax.all_to_all(send, "expert", split_axis=0, concat_axis=0, tiled=True)
    gate_acts = jnp.einsum("scd,df->scf", arrived, w_gate, preferred_element_type=jnp.float32)
    up_acts = jnp.einsum("scd,df->scf", arrived, w_up, preferred_element_type=jnp.float32)
    hidden_acts = (jax.nn.silu(gate_acts) * up_acts).astype(jnp.bfloat16)
    partial_value = jnp.einsum("scf,fd->scd", hidden_acts, w_down, preferred_element_type=jnp.float32)
    summed = lax.psum_scatter(
        partial_value.astype(jnp.bfloat16), "hidden", scatter_dimension=2, tiled=True
    )
    return lax.all_to_all(summed, "expert", split_axis=0, concat_axis=0, tiled=True)


def body(tokens, w_gate, w_up, w_down, routes, gate_levels, ancestors):
    local_rows = routes.shape[0]
    choose = routes.shape[1]
    groups = lax.axis_size("expert")
    local_experts = w_gate.shape[0]
    experts = local_experts * groups
    capacity = 3 * local_rows * choose // (2 * experts)
    pairs = local_rows * choose
    chosen = routes.reshape(-1)
    one_hot = (chosen[:, None] == jnp.arange(experts, dtype=jnp.int32)[None, :]).astype(jnp.bfloat16)
    lower = jnp.arange(pairs, dtype=jnp.int32)
    tri = (lower[:, None] > lower[None, :]).astype(jnp.bfloat16)
    earlier = jnp.dot(tri, one_hot, preferred_element_type=jnp.float32)
    places = jnp.sum(earlier * one_hot.astype(jnp.float32), 1).astype(jnp.int32)
    target = chosen * capacity + places
    row_ids = jnp.arange(pairs, dtype=jnp.int32) // choose
    slot_rows = jnp.zeros((experts * capacity,), jnp.int32).at[target].set(row_ids)
    slot_rows = slot_rows.reshape(groups, local_experts, capacity)
    whole_rows = lax.all_gather(tokens, "hidden", axis=1, tiled=True)
    piece = capacity // SPLIT
    per_expert = []
    for c in range(local_experts):
        parts = []
        for p in range(SPLIT):
            send = whole_rows[slot_rows[:, c, p * piece:(p + 1) * piece]]
            parts.append(expert_chunk(send, w_gate[c], w_up[c], w_down[c]))
        per_expert.append(jnp.concatenate(parts, 1) if SPLIT > 1 else parts[0])
    returned = jnp.stack(per_expert, 1)
    returned = returned.reshape(experts * capacity, returned.shape[3])
    source = target.reshape(local_rows, choose)[ancestors]
    levels = gate_levels.astype(jnp.float32)[ancestors]
    weights = levels / jnp.sum(levels, 1, keepdims=True)
    picked = returned[source].astype(jnp.float32)
    combined = jnp.sum(weights[:, :, None] * picked, 1)
    return combined.astype(jnp.bfloat16)


def solution(mesh):
    placed = (
        P("expert", "hidden"),
        P("expert", None, "hidden"),
        P("expert", None, "hidden"),
        P("expert", "hidden", None),
        P("expert", None),
        P("expert", None),
        P("expert"),
    )
    return jax.shard_map(
        body, mesh=mesh, in_specs=placed, out_specs=P("expert", "hidden"), check_vma=False
    )
```

```python
import jax
import jax.numpy as jnp
from jax import lax
from jax.sharding import PartitionSpec as P

def expert_part(arrived, w_gate, w_up, w_down):
    gate_acts = jnp.einsum("scd,df->scf", arrived, w_gate, preferred_element_type=jnp.float32)
    up_acts = jnp.einsum("scd,df->scf", arrived, w_up, preferred_element_type=jnp.float32)
    hidden_acts = (jax.nn.silu(gate_acts) * up_acts).astype(jnp.bfloat16)
    partial_value = jnp.einsum("scf,fd->scd", hidden_acts, w_down, preferred_element_type=jnp.float32)
    return partial_value.astype(jnp.bfloat16)


def body(tokens, w_gate, w_up, w_down, routes, gate_levels, ancestors):
    local_rows = routes.shape[0]
    choose = routes.shape[1]
    groups = lax.axis_size("expert")
    local_experts = w_gate.shape[0]
    experts = local_experts * groups
    capacity = 3 * local_rows * choose // (2 * experts)
    pairs = local_rows * choose
    chosen = routes.reshape(-1)
    one_hot = (chosen[:, None] == jnp.arange(experts, dtype=jnp.int32)[None, :]).astype(jnp.bfloat16)
    lower = jnp.arange(pairs, dtype=jnp.int32)
    tri = (lower[:, None] > lower[None, :]).astype(jnp.bfloat16)
    earlier = jnp.dot(tri, one_hot, preferred_element_type=jnp.float32)
    places = jnp.sum(earlier * one_hot.astype(jnp.float32), 1).astype(jnp.int32)
    target = chosen * capacity + places
    row_ids = jnp.arange(pairs, dtype=jnp.int32) // choose
    slot_rows = jnp.zeros((experts * capacity,), jnp.int32).at[target].set(row_ids)
    slot_rows = slot_rows.reshape(groups, local_experts, capacity)
    whole_rows = lax.all_gather(tokens, "hidden", axis=1, tiled=True)
    lead = capacity // 2
    send0 = whole_rows[jnp.concatenate([slot_rows[:, 0], slot_rows[:, 1, :lead]], 1)]
    send1 = whole_rows[slot_rows[:, 1, lead:]]
    arrived0 = lax.all_to_all(send0, "expert", split_axis=0, concat_axis=0, tiled=True)
    part0 = jnp.concatenate(
        [expert_part(arrived0[:, :capacity], w_gate[0], w_up[0], w_down[0]),
         expert_part(arrived0[:, capacity:], w_gate[1], w_up[1], w_down[1])], 1)
    summed0 = lax.psum_scatter(part0, "hidden", scatter_dimension=2, tiled=True)
    arrived1 = lax.all_to_all(send1, "expert", split_axis=0, concat_axis=0, tiled=True)
    part1 = expert_part(arrived1, w_gate[1], w_up[1], w_down[1])
    summed1 = lax.psum_scatter(part1, "hidden", scatter_dimension=2, tiled=True)
    back0 = lax.all_to_all(summed0, "expert", split_axis=0, concat_axis=0, tiled=True)
    back1 = lax.all_to_all(summed1, "expert", split_axis=0, concat_axis=0, tiled=True)
    per_expert = [back0[:, :capacity], jnp.concatenate([back0[:, capacity:], back1], 1)]
    returned = jnp.stack(per_expert, 1)
    returned = returned.reshape(experts * capacity, returned.shape[3])
    source = target.reshape(local_rows, choose)[ancestors]
    levels = gate_levels.astype(jnp.float32)[ancestors]
    weights = levels / jnp.sum(levels, 1, keepdims=True)
    picked = returned[source].astype(jnp.float32)
    combined = jnp.sum(weights[:, :, None] * picked, 1)
    return combined.astype(jnp.bfloat16)


def solution(mesh):
    placed = (
        P("expert", "hidden"),
        P("expert", None, "hidden"),
        P("expert", None, "hidden"),
        P("expert", "hidden", None),
        P("expert", None),
        P("expert", None),
        P("expert"),
    )
    return jax.shard_map(
        body, mesh=mesh, in_specs=placed, out_specs=P("expert", "hidden"), check_vma=False
    )
```

```python
import jax
import jax.numpy as jnp
from jax import lax
from jax.sharding import PartitionSpec as P

def expert_part(arrived, w_gate, w_up, w_down):
    gate_acts = jnp.einsum("scd,df->scf", arrived, w_gate, preferred_element_type=jnp.float32)
    up_acts = jnp.einsum("scd,df->scf", arrived, w_up, preferred_element_type=jnp.float32)
    hidden_acts = (jax.nn.silu(gate_acts) * up_acts).astype(jnp.bfloat16)
    partial_value = jnp.einsum("scf,fd->scd", hidden_acts, w_down, preferred_element_type=jnp.float32)
    return partial_value.astype(jnp.bfloat16)


def body(tokens, w_gate, w_up, w_down, routes, gate_levels, ancestors):
    local_rows = routes.shape[0]
    choose = routes.shape[1]
    groups = lax.axis_size("expert")
    local_experts = w_gate.shape[0]
    experts = local_experts * groups
    capacity = 3 * local_rows * choose // (2 * experts)
    pairs = local_rows * choose
    chosen = routes.reshape(-1)
    one_hot = (chosen[:, None] == jnp.arange(experts, dtype=jnp.int32)[None, :]).astype(jnp.bfloat16)
    lower = jnp.arange(pairs, dtype=jnp.int32)
    tri = (lower[:, None] > lower[None, :]).astype(jnp.bfloat16)
    earlier = jnp.dot(tri, one_hot, preferred_element_type=jnp.float32)
    places = jnp.sum(earlier * one_hot.astype(jnp.float32), 1).astype(jnp.int32)
    target = chosen * capacity + places
    row_ids = jnp.arange(pairs, dtype=jnp.int32) // choose
    slot_rows = jnp.zeros((experts * capacity,), jnp.int32).at[target].set(row_ids)
    slot_rows = slot_rows.reshape(groups, local_experts, capacity)
    per_expert = []
    for c in range(local_experts):
        send = tokens[slot_rows[:, c]]
        arrived = lax.all_to_all(send, "expert", split_axis=0, concat_axis=0, tiled=True)
        full = lax.all_gather(arrived, "hidden", axis=2, tiled=True)
        part = expert_part(full, w_gate[c], w_up[c], w_down[c])
        summed = lax.psum_scatter(part, "hidden", scatter_dimension=2, tiled=True)
        per_expert.append(lax.all_to_all(summed, "expert", split_axis=0, concat_axis=0, tiled=True))
    returned = jnp.stack(per_expert, 1)
    returned = returned.reshape(experts * capacity, returned.shape[3])
    source = target.reshape(local_rows, choose)[ancestors]
    levels = gate_levels.astype(jnp.float32)[ancestors]
    weights = levels / jnp.sum(levels, 1, keepdims=True)
    picked = returned[source].astype(jnp.float32)
    combined = jnp.sum(weights[:, :, None] * picked, 1)
    return combined.astype(jnp.bfloat16)


def solution(mesh):
    placed = (
        P("expert", "hidden"),
        P("expert", None, "hidden"),
        P("expert", None, "hidden"),
        P("expert", "hidden", None),
        P("expert", None),
        P("expert", None),
        P("expert"),
    )
    return jax.shard_map(
        body, mesh=mesh, in_specs=placed, out_specs=P("expert", "hidden"), check_vma=False
    )
```

```python
import jax
import jax.numpy as jnp
from jax import lax
from jax.sharding import PartitionSpec as P

def expert_part(arrived, w_gate, w_up, w_down):
    gate_acts = jnp.einsum("scd,df->scf", arrived, w_gate, preferred_element_type=jnp.float32)
    up_acts = jnp.einsum("scd,df->scf", arrived, w_up, preferred_element_type=jnp.float32)
    hidden_acts = (jax.nn.silu(gate_acts) * up_acts).astype(jnp.bfloat16)
    partial_value = jnp.einsum("scf,fd->scd", hidden_acts, w_down, preferred_element_type=jnp.float32)
    return partial_value.astype(jnp.bfloat16)


def gather_hidden(piece):
    size = lax.axis_size("hidden")
    here = lax.axis_index("hidden")
    shifted = [piece] + [
        lax.ppermute(piece, "hidden", [(i, (i + k) % size) for i in range(size)])
        for k in range(1, size)
    ]
    order = (here - jnp.arange(size, dtype=jnp.int32)) % size
    stacked = jnp.take(jnp.stack(shifted, 0), order, axis=0)
    return jnp.moveaxis(stacked, 0, -2).reshape(piece.shape[:-1] + (size * piece.shape[-1],))


def body(tokens, w_gate, w_up, w_down, routes, gate_levels, ancestors):
    local_rows = routes.shape[0]
    choose = routes.shape[1]
    groups = lax.axis_size("expert")
    local_experts = w_gate.shape[0]
    experts = local_experts * groups
    capacity = 3 * local_rows * choose // (2 * experts)
    pairs = local_rows * choose
    chosen = routes.reshape(-1)
    one_hot = (chosen[:, None] == jnp.arange(experts, dtype=jnp.int32)[None, :]).astype(jnp.bfloat16)
    lower = jnp.arange(pairs, dtype=jnp.int32)
    tri = (lower[:, None] > lower[None, :]).astype(jnp.bfloat16)
    earlier = jnp.dot(tri, one_hot, preferred_element_type=jnp.float32)
    places = jnp.sum(earlier * one_hot.astype(jnp.float32), 1).astype(jnp.int32)
    target = chosen * capacity + places
    row_ids = jnp.arange(pairs, dtype=jnp.int32) // choose
    slot_rows = jnp.zeros((experts * capacity,), jnp.int32).at[target].set(row_ids)
    slot_rows = slot_rows.reshape(groups, local_experts, capacity)
    per_expert = []
    for c in range(local_experts):
        send = tokens[slot_rows[:, c]]
        arrived = lax.all_to_all(send, "expert", split_axis=0, concat_axis=0, tiled=True)
        full = gather_hidden(arrived)
        part = expert_part(full, w_gate[c], w_up[c], w_down[c])
        summed = lax.psum_scatter(part, "hidden", scatter_dimension=2, tiled=True)
        per_expert.append(lax.all_to_all(summed, "expert", split_axis=0, concat_axis=0, tiled=True))
    returned = jnp.stack(per_expert, 1)
    returned = returned.reshape(experts * capacity, returned.shape[3])
    source = target.reshape(local_rows, choose)[ancestors]
    levels = gate_levels.astype(jnp.float32)[ancestors]
    weights = levels / jnp.sum(levels, 1, keepdims=True)
    picked = returned[source].astype(jnp.float32)
    combined = jnp.sum(weights[:, :, None] * picked, 1)
    return combined.astype(jnp.bfloat16)


def solution(mesh):
    placed = (
        P("expert", "hidden"),
        P("expert", None, "hidden"),
        P("expert", None, "hidden"),
        P("expert", "hidden", None),
        P("expert", None),
        P("expert", None),
        P("expert"),
    )
    return jax.shard_map(
        body, mesh=mesh, in_specs=placed, out_specs=P("expert", "hidden"), check_vma=False
    )
```

```python
import jax
import jax.numpy as jnp
from jax import lax
from jax.sharding import PartitionSpec as P

def expert_part(arrived, w_gate, w_up, w_down):
    gate_acts = jnp.einsum("scd,df->scf", arrived, w_gate, preferred_element_type=jnp.float32)
    up_acts = jnp.einsum("scd,df->scf", arrived, w_up, preferred_element_type=jnp.float32)
    hidden_acts = (jax.nn.silu(gate_acts) * up_acts).astype(jnp.bfloat16)
    partial_value = jnp.einsum("scf,fd->scd", hidden_acts, w_down, preferred_element_type=jnp.float32)
    return partial_value.astype(jnp.bfloat16)


def body(tokens, w_gate, w_up, w_down, routes, gate_levels, ancestors):
    local_rows = routes.shape[0]
    choose = routes.shape[1]
    groups = lax.axis_size("expert")
    local_experts = w_gate.shape[0]
    experts = local_experts * groups
    capacity = 3 * local_rows * choose // (2 * experts)
    pairs = local_rows * choose
    chosen = routes.reshape(-1)
    one_hot = (chosen[:, None] == jnp.arange(experts, dtype=jnp.int32)[None, :]).astype(jnp.bfloat16)
    lower = jnp.arange(pairs, dtype=jnp.int32)
    tri = (lower[:, None] > lower[None, :]).astype(jnp.bfloat16)
    earlier = jnp.dot(tri, one_hot, preferred_element_type=jnp.float32)
    places = jnp.sum(earlier * one_hot.astype(jnp.float32), 1).astype(jnp.int32)
    target = chosen * capacity + places
    row_ids = jnp.arange(pairs, dtype=jnp.int32) // choose
    slot_rows = jnp.zeros((experts * capacity,), jnp.int32).at[target].set(row_ids)
    slot_rows = slot_rows.reshape(groups, local_experts, capacity)
    arrived = lax.all_to_all(tokens[slot_rows[:, 0]], "expert", split_axis=0, concat_axis=0, tiled=True)
    full0 = lax.all_gather(arrived, "hidden", axis=2, tiled=True)
    whole_rows = lax.all_gather(tokens, "hidden", axis=1, tiled=True)
    full1 = lax.all_to_all(whole_rows[slot_rows[:, 1]], "expert", split_axis=0, concat_axis=0, tiled=True)
    per_expert = []
    for c, full in enumerate((full0, full1)):
        part = expert_part(full, w_gate[c], w_up[c], w_down[c])
        summed = lax.psum_scatter(part, "hidden", scatter_dimension=2, tiled=True)
        per_expert.append(lax.all_to_all(summed, "expert", split_axis=0, concat_axis=0, tiled=True))
    returned = jnp.stack(per_expert, 1)
    returned = returned.reshape(experts * capacity, returned.shape[3])
    source = target.reshape(local_rows, choose)[ancestors]
    levels = gate_levels.astype(jnp.float32)[ancestors]
    weights = levels / jnp.sum(levels, 1, keepdims=True)
    picked = returned[source].astype(jnp.float32)
    combined = jnp.sum(weights[:, :, None] * picked, 1)
    return combined.astype(jnp.bfloat16)


def solution(mesh):
    placed = (
        P("expert", "hidden"),
        P("expert", None, "hidden"),
        P("expert", None, "hidden"),
        P("expert", "hidden", None),
        P("expert", None),
        P("expert", None),
        P("expert"),
    )
    return jax.shard_map(
        body, mesh=mesh, in_specs=placed, out_specs=P("expert", "hidden"), check_vma=False
    )
```

```python
import jax
import jax.numpy as jnp
from jax import lax
from jax.sharding import PartitionSpec as P

def expert_part(arrived, w_gate, w_up, w_down):
    gate_acts = jnp.einsum("scd,df->scf", arrived, w_gate, preferred_element_type=jnp.float32)
    up_acts = jnp.einsum("scd,df->scf", arrived, w_up, preferred_element_type=jnp.float32)
    hidden_acts = (jax.nn.silu(gate_acts) * up_acts).astype(jnp.bfloat16)
    partial_value = jnp.einsum("scf,fd->scd", hidden_acts, w_down, preferred_element_type=jnp.float32)
    return partial_value.astype(jnp.bfloat16)


def body(tokens, w_gate, w_up, w_down, routes, gate_levels, ancestors):
    local_rows = routes.shape[0]
    choose = routes.shape[1]
    groups = lax.axis_size("expert")
    local_experts = w_gate.shape[0]
    experts = local_experts * groups
    capacity = 3 * local_rows * choose // (2 * experts)
    pairs = local_rows * choose
    chosen = routes.reshape(-1)
    one_hot = (chosen[:, None] == jnp.arange(experts, dtype=jnp.int32)[None, :]).astype(jnp.bfloat16)
    lower = jnp.arange(pairs, dtype=jnp.int32)
    tri = (lower[:, None] > lower[None, :]).astype(jnp.bfloat16)
    earlier = jnp.dot(tri, one_hot, preferred_element_type=jnp.float32)
    places = jnp.sum(earlier * one_hot.astype(jnp.float32), 1).astype(jnp.int32)
    target = chosen * capacity + places
    row_ids = jnp.arange(pairs, dtype=jnp.int32) // choose
    slot_rows = jnp.zeros((experts * capacity,), jnp.int32).at[target].set(row_ids)
    slot_rows = slot_rows.reshape(groups, local_experts, capacity)
    arrived = lax.all_to_all(tokens[slot_rows[:, 0]], "expert", split_axis=0, concat_axis=0, tiled=True)
    full0 = lax.all_gather(arrived, "hidden", axis=2, tiled=True)
    whole_rows = lax.all_gather(tokens, "hidden", axis=1, tiled=True)
    lead = capacity // 2
    head = lax.all_to_all(whole_rows[slot_rows[:, 1, :lead]], "expert", split_axis=0, concat_axis=0, tiled=True)
    full0, head = lax.optimization_barrier((full0, head))
    part0 = expert_part(full0, w_gate[0], w_up[0], w_down[0])
    summed0 = lax.psum_scatter(part0, "hidden", scatter_dimension=2, tiled=True)
    tail_rows, part0 = lax.optimization_barrier((slot_rows[:, 1, lead:], part0))
    tail = lax.all_to_all(whole_rows[tail_rows], "expert", split_axis=0, concat_axis=0, tiled=True)
    part1 = expert_part(jnp.concatenate([head, tail], 1), w_gate[1], w_up[1], w_down[1])
    summed1 = lax.psum_scatter(part1, "hidden", scatter_dimension=2, tiled=True)
    per_expert = [lax.all_to_all(s, "expert", split_axis=0, concat_axis=0, tiled=True) for s in (summed0, summed1)]
    returned = jnp.stack(per_expert, 1)
    returned = returned.reshape(experts * capacity, returned.shape[3])
    source = target.reshape(local_rows, choose)[ancestors]
    levels = gate_levels.astype(jnp.float32)[ancestors]
    weights = levels / jnp.sum(levels, 1, keepdims=True)
    picked = returned[source].astype(jnp.float32)
    combined = jnp.sum(weights[:, :, None] * picked, 1)
    return combined.astype(jnp.bfloat16)


def solution(mesh):
    placed = (
        P("expert", "hidden"),
        P("expert", None, "hidden"),
        P("expert", None, "hidden"),
        P("expert", "hidden", None),
        P("expert", None),
        P("expert", None),
        P("expert"),
    )
    return jax.shard_map(
        body, mesh=mesh, in_specs=placed, out_specs=P("expert", "hidden"), check_vma=False
    )
```

```python
import jax
import jax.numpy as jnp
from jax import lax
from jax.sharding import PartitionSpec as P

def expert_part(arrived, w_gate, w_up, w_down):
    gate_acts = jnp.einsum("scd,df->scf", arrived, w_gate, preferred_element_type=jnp.float32)
    up_acts = jnp.einsum("scd,df->scf", arrived, w_up, preferred_element_type=jnp.float32)
    hidden_acts = (jax.nn.silu(gate_acts) * up_acts).astype(jnp.bfloat16)
    partial_value = jnp.einsum("scf,fd->scd", hidden_acts, w_down, preferred_element_type=jnp.float32)
    return partial_value.astype(jnp.bfloat16)


def body(tokens, w_gate, w_up, w_down, routes, gate_levels, ancestors):
    local_rows = routes.shape[0]
    choose = routes.shape[1]
    groups = lax.axis_size("expert")
    local_experts = w_gate.shape[0]
    experts = local_experts * groups
    capacity = 3 * local_rows * choose // (2 * experts)
    pairs = local_rows * choose
    chosen = routes.reshape(-1)
    one_hot = (chosen[:, None] == jnp.arange(experts, dtype=jnp.int32)[None, :]).astype(jnp.bfloat16)
    lower = jnp.arange(pairs, dtype=jnp.int32)
    tri = (lower[:, None] > lower[None, :]).astype(jnp.bfloat16)
    earlier = jnp.dot(tri, one_hot, preferred_element_type=jnp.float32)
    places = jnp.sum(earlier * one_hot.astype(jnp.float32), 1).astype(jnp.int32)
    target = chosen * capacity + places
    row_ids = jnp.arange(pairs, dtype=jnp.int32) // choose
    slot_rows = jnp.zeros((experts * capacity,), jnp.int32).at[target].set(row_ids)
    slot_rows = slot_rows.reshape(groups, local_experts, capacity)
    arrived = lax.all_to_all(tokens[slot_rows[:, 0]], "expert", split_axis=0, concat_axis=0, tiled=True)
    full0 = lax.all_gather(arrived, "hidden", axis=2, tiled=True)
    whole_rows = lax.all_gather(tokens, "hidden", axis=1, tiled=True)
    lead = 2 * capacity // 3
    head = lax.all_to_all(whole_rows[slot_rows[:, 1, :lead]], "expert", split_axis=0, concat_axis=0, tiled=True)
    full0, head = lax.optimization_barrier((full0, head))
    part0 = expert_part(full0, w_gate[0], w_up[0], w_down[0])
    summed0 = lax.psum_scatter(part0, "hidden", scatter_dimension=2, tiled=True)
    tail_rows, part0 = lax.optimization_barrier((slot_rows[:, 1, lead:], part0))
    tail = lax.all_to_all(whole_rows[tail_rows], "expert", split_axis=0, concat_axis=0, tiled=True)
    part1 = expert_part(jnp.concatenate([head, tail], 1), w_gate[1], w_up[1], w_down[1])
    summed1 = lax.psum_scatter(part1, "hidden", scatter_dimension=2, tiled=True)
    per_expert = [lax.all_to_all(s, "expert", split_axis=0, concat_axis=0, tiled=True) for s in (summed0, summed1)]
    returned = jnp.stack(per_expert, 1)
    returned = returned.reshape(experts * capacity, returned.shape[3])
    source = target.reshape(local_rows, choose)[ancestors]
    levels = gate_levels.astype(jnp.float32)[ancestors]
    weights = levels / jnp.sum(levels, 1, keepdims=True)
    picked = returned[source].astype(jnp.float32)
    combined = jnp.sum(weights[:, :, None] * picked, 1)
    return combined.astype(jnp.bfloat16)


def solution(mesh):
    placed = (
        P("expert", "hidden"),
        P("expert", None, "hidden"),
        P("expert", None, "hidden"),
        P("expert", "hidden", None),
        P("expert", None),
        P("expert", None),
        P("expert"),
    )
    return jax.shard_map(
        body, mesh=mesh, in_specs=placed, out_specs=P("expert", "hidden"), check_vma=False
    )
```

```python
import jax
import jax.numpy as jnp
from jax import lax
from jax.sharding import PartitionSpec as P

def expert_part(arrived, w_gate, w_up, w_down):
    gate_acts = jnp.einsum("scd,df->scf", arrived, w_gate, preferred_element_type=jnp.float32)
    up_acts = jnp.einsum("scd,df->scf", arrived, w_up, preferred_element_type=jnp.float32)
    hidden_acts = (jax.nn.silu(gate_acts) * up_acts).astype(jnp.bfloat16)
    partial_value = jnp.einsum("scf,fd->scd", hidden_acts, w_down, preferred_element_type=jnp.float32)
    return partial_value.astype(jnp.bfloat16)


def body(tokens, w_gate, w_up, w_down, routes, gate_levels, ancestors):
    local_rows = routes.shape[0]
    choose = routes.shape[1]
    groups = lax.axis_size("expert")
    local_experts = w_gate.shape[0]
    experts = local_experts * groups
    capacity = 3 * local_rows * choose // (2 * experts)
    pairs = local_rows * choose
    chosen = routes.reshape(-1)
    one_hot = (chosen[:, None] == jnp.arange(experts, dtype=jnp.int32)[None, :]).astype(jnp.bfloat16)
    lower = jnp.arange(pairs, dtype=jnp.int32)
    tri = (lower[:, None] > lower[None, :]).astype(jnp.bfloat16)
    earlier = jnp.dot(tri, one_hot, preferred_element_type=jnp.float32)
    places = jnp.sum(earlier * one_hot.astype(jnp.float32), 1).astype(jnp.int32)
    target = chosen * capacity + places
    row_ids = jnp.arange(pairs, dtype=jnp.int32) // choose
    picks = (target[:, None] == jnp.arange(experts * capacity, dtype=jnp.int32)[None, :]).astype(jnp.bfloat16)
    slot_rows = jnp.dot(row_ids.astype(jnp.bfloat16), picks, preferred_element_type=jnp.float32).astype(jnp.int32)
    slot_rows = slot_rows.reshape(groups, local_experts, capacity)
    arrived = lax.all_to_all(tokens[slot_rows[:, 0]], "expert", split_axis=0, concat_axis=0, tiled=True)
    full0 = lax.all_gather(arrived, "hidden", axis=2, tiled=True)
    whole_rows = lax.all_gather(tokens, "hidden", axis=1, tiled=True)
    lead = 2 * capacity // 3
    head = lax.all_to_all(whole_rows[slot_rows[:, 1, :lead]], "expert", split_axis=0, concat_axis=0, tiled=True)
    full0, head = lax.optimization_barrier((full0, head))
    part0 = expert_part(full0, w_gate[0], w_up[0], w_down[0])
    summed0 = lax.psum_scatter(part0, "hidden", scatter_dimension=2, tiled=True)
    tail_rows, part0 = lax.optimization_barrier((slot_rows[:, 1, lead:], part0))
    tail = lax.all_to_all(whole_rows[tail_rows], "expert", split_axis=0, concat_axis=0, tiled=True)
    part1 = expert_part(jnp.concatenate([head, tail], 1), w_gate[1], w_up[1], w_down[1])
    summed1 = lax.psum_scatter(part1, "hidden", scatter_dimension=2, tiled=True)
    per_expert = [lax.all_to_all(s, "expert", split_axis=0, concat_axis=0, tiled=True) for s in (summed0, summed1)]
    returned = jnp.stack(per_expert, 1)
    returned = returned.reshape(experts * capacity, returned.shape[3])
    source = target.reshape(local_rows, choose)[ancestors]
    levels = gate_levels.astype(jnp.float32)[ancestors]
    weights = levels / jnp.sum(levels, 1, keepdims=True)
    picked = returned[source].astype(jnp.float32)
    combined = jnp.sum(weights[:, :, None] * picked, 1)
    return combined.astype(jnp.bfloat16)


def solution(mesh):
    placed = (
        P("expert", "hidden"),
        P("expert", None, "hidden"),
        P("expert", None, "hidden"),
        P("expert", "hidden", None),
        P("expert", None),
        P("expert", None),
        P("expert"),
    )
    return jax.shard_map(
        body, mesh=mesh, in_specs=placed, out_specs=P("expert", "hidden"), check_vma=False
    )
```

```python
import jax
import jax.numpy as jnp
from jax import lax
from jax.sharding import PartitionSpec as P

def expert_part(arrived, w_gate, w_up, w_down):
    gate_acts = jnp.einsum("scd,df->scf", arrived, w_gate, preferred_element_type=jnp.float32)
    up_acts = jnp.einsum("scd,df->scf", arrived, w_up, preferred_element_type=jnp.float32)
    hidden_acts = (jax.nn.silu(gate_acts) * up_acts).astype(jnp.bfloat16)
    partial_value = jnp.einsum("scf,fd->scd", hidden_acts, w_down, preferred_element_type=jnp.float32)
    return partial_value.astype(jnp.bfloat16)


def reduce_hidden(part):
    size = lax.axis_size("hidden")
    quarters = part.reshape(part.shape[:-1] + (size, part.shape[-1] // size))
    quarters = jnp.moveaxis(quarters, -2, 0)
    gathered = lax.all_to_all(quarters, "hidden", split_axis=0, concat_axis=0, tiled=True)
    return jnp.sum(gathered.astype(jnp.float32), 0).astype(jnp.bfloat16)


def body(tokens, w_gate, w_up, w_down, routes, gate_levels, ancestors):
    local_rows = routes.shape[0]
    choose = routes.shape[1]
    groups = lax.axis_size("expert")
    local_experts = w_gate.shape[0]
    experts = local_experts * groups
    capacity = 3 * local_rows * choose // (2 * experts)
    pairs = local_rows * choose
    chosen = routes.reshape(-1)
    one_hot = (chosen[:, None] == jnp.arange(experts, dtype=jnp.int32)[None, :]).astype(jnp.bfloat16)
    lower = jnp.arange(pairs, dtype=jnp.int32)
    tri = (lower[:, None] > lower[None, :]).astype(jnp.bfloat16)
    earlier = jnp.dot(tri, one_hot, preferred_element_type=jnp.float32)
    places = jnp.sum(earlier * one_hot.astype(jnp.float32), 1).astype(jnp.int32)
    target = chosen * capacity + places
    row_ids = jnp.arange(pairs, dtype=jnp.int32) // choose
    picks = (target[:, None] == jnp.arange(experts * capacity, dtype=jnp.int32)[None, :]).astype(jnp.bfloat16)
    slot_rows = jnp.dot(row_ids.astype(jnp.bfloat16), picks, preferred_element_type=jnp.float32).astype(jnp.int32)
    slot_rows = slot_rows.reshape(groups, local_experts, capacity)
    arrived = lax.all_to_all(tokens[slot_rows[:, 0]], "expert", split_axis=0, concat_axis=0, tiled=True)
    full0 = lax.all_gather(arrived, "hidden", axis=2, tiled=True)
    whole_rows = lax.all_gather(tokens, "hidden", axis=1, tiled=True)
    lead = 2 * capacity // 3
    head = lax.all_to_all(whole_rows[slot_rows[:, 1, :lead]], "expert", split_axis=0, concat_axis=0, tiled=True)
    full0, head = lax.optimization_barrier((full0, head))
    part0 = expert_part(full0, w_gate[0], w_up[0], w_down[0])
    summed0 = lax.psum_scatter(part0, "hidden", scatter_dimension=2, tiled=True)
    tail_rows, part0 = lax.optimization_barrier((slot_rows[:, 1, lead:], part0))
    tail = lax.all_to_all(whole_rows[tail_rows], "expert", split_axis=0, concat_axis=0, tiled=True)
    part_head = expert_part(head, w_gate[1], w_up[1], w_down[1])
    summed_head = lax.psum_scatter(part_head, "hidden", scatter_dimension=2, tiled=True)
    part_tail = expert_part(tail, w_gate[1], w_up[1], w_down[1])
    summed_tail = reduce_hidden(part_tail)
    summed1 = jnp.concatenate([summed_head, summed_tail], 1)
    per_expert = [lax.all_to_all(s, "expert", split_axis=0, concat_axis=0, tiled=True) for s in (summed0, summed1)]
    returned = jnp.stack(per_expert, 1)
    returned = returned.reshape(experts * capacity, returned.shape[3])
    source = target.reshape(local_rows, choose)[ancestors]
    levels = gate_levels.astype(jnp.float32)[ancestors]
    weights = levels / jnp.sum(levels, 1, keepdims=True)
    picked = returned[source].astype(jnp.float32)
    combined = jnp.sum(weights[:, :, None] * picked, 1)
    return combined.astype(jnp.bfloat16)


def solution(mesh):
    placed = (
        P("expert", "hidden"),
        P("expert", None, "hidden"),
        P("expert", None, "hidden"),
        P("expert", "hidden", None),
        P("expert", None),
        P("expert", None),
        P("expert"),
    )
    return jax.shard_map(
        body, mesh=mesh, in_specs=placed, out_specs=P("expert", "hidden"), check_vma=False
    )
```

```python
import jax
import jax.numpy as jnp
from jax import lax
from jax.sharding import PartitionSpec as P

def expert_part(arrived, w_gate, w_up, w_down):
    gate_acts = jnp.einsum("scd,df->scf", arrived, w_gate, preferred_element_type=jnp.float32)
    up_acts = jnp.einsum("scd,df->scf", arrived, w_up, preferred_element_type=jnp.float32)
    hidden_acts = (jax.nn.silu(gate_acts) * up_acts).astype(jnp.bfloat16)
    partial_value = jnp.einsum("scf,fd->scd", hidden_acts, w_down, preferred_element_type=jnp.float32)
    return partial_value.astype(jnp.bfloat16)


def body(tokens, w_gate, w_up, w_down, routes, gate_levels, ancestors):
    local_rows = routes.shape[0]
    choose = routes.shape[1]
    groups = lax.axis_size("expert")
    local_experts = w_gate.shape[0]
    experts = local_experts * groups
    capacity = 3 * local_rows * choose // (2 * experts)
    pairs = local_rows * choose
    chosen = routes.reshape(-1)
    one_hot = (chosen[:, None] == jnp.arange(experts, dtype=jnp.int32)[None, :]).astype(jnp.bfloat16)
    lower = jnp.arange(pairs, dtype=jnp.int32)
    tri = (lower[:, None] > lower[None, :]).astype(jnp.bfloat16)
    earlier = jnp.dot(tri, one_hot, preferred_element_type=jnp.float32)
    places = jnp.sum(earlier * one_hot.astype(jnp.float32), 1).astype(jnp.int32)
    target = chosen * capacity + places
    row_ids = jnp.arange(pairs, dtype=jnp.int32) // choose
    picks = (target[:, None] == jnp.arange(experts * capacity, dtype=jnp.int32)[None, :]).astype(jnp.bfloat16)
    slot_rows = jnp.dot(row_ids.astype(jnp.bfloat16), picks, preferred_element_type=jnp.float32).astype(jnp.int32)
    slot_rows = slot_rows.reshape(groups, local_experts, capacity)
    arrived = lax.all_to_all(tokens[slot_rows[:, 0]], "expert", split_axis=0, concat_axis=0, tiled=True)
    full0 = lax.all_gather(arrived, "hidden", axis=2, tiled=True)
    whole_rows = lax.all_gather(tokens, "hidden", axis=1, tiled=True)
    lead = 2 * capacity // 3
    head = lax.all_to_all(whole_rows[slot_rows[:, 1, :lead]], "expert", split_axis=0, concat_axis=0, tiled=True)
    full0, head = lax.optimization_barrier((full0, head))
    part0 = expert_part(full0, w_gate[0], w_up[0], w_down[0])
    summed0 = lax.psum_scatter(part0, "hidden", scatter_dimension=2, tiled=True)
    tail_rows, part0 = lax.optimization_barrier((slot_rows[:, 1, lead:], part0))
    tail = lax.all_to_all(whole_rows[tail_rows], "expert", split_axis=0, concat_axis=0, tiled=True)
    part1 = expert_part(jnp.concatenate([head, tail], 1), w_gate[1], w_up[1], w_down[1])
    summed1 = lax.psum_scatter(part1, "hidden", scatter_dimension=2, tiled=True)
    per_expert = [lax.all_to_all(s, "expert", split_axis=0, concat_axis=0, tiled=True) for s in (summed0, summed1)]
    source = target.reshape(local_rows, choose)[ancestors]
    levels = gate_levels.astype(jnp.float32)[ancestors]
    weights = levels / jnp.sum(levels, 1, keepdims=True)
    slots = jnp.arange(experts * capacity, dtype=jnp.int32)
    mixing = jnp.sum(jnp.where(source[:, :, None] == slots[None, None, :], weights[:, :, None], 0.0), 1)
    mixing = mixing.reshape(local_rows, groups, local_experts, capacity)
    combined = sum(
        jnp.dot(
            mixing[:, :, c].reshape(local_rows, groups * capacity),
            back.reshape(groups * capacity, back.shape[2]).astype(jnp.float32),
            precision=lax.Precision.HIGHEST,
        )
        for c, back in enumerate(per_expert)
    )
    return combined.astype(jnp.bfloat16)


def solution(mesh):
    placed = (
        P("expert", "hidden"),
        P("expert", None, "hidden"),
        P("expert", None, "hidden"),
        P("expert", "hidden", None),
        P("expert", None),
        P("expert", None),
        P("expert"),
    )
    return jax.shard_map(
        body, mesh=mesh, in_specs=placed, out_specs=P("expert", "hidden"), check_vma=False
    )
```

```python
import jax
import jax.numpy as jnp
from jax import lax
from jax.sharding import PartitionSpec as P

def expert_part(arrived, w_gate, w_up, w_down):
    if arrived.ndim == 4:
        quarters = arrived.shape[0]
        w_gate = w_gate.reshape(quarters, w_gate.shape[0] // quarters, w_gate.shape[1])
        w_up = w_up.reshape(quarters, w_up.shape[0] // quarters, w_up.shape[1])
        gate_acts = jnp.einsum("qscd,qdf->scf", arrived, w_gate, preferred_element_type=jnp.float32)
        up_acts = jnp.einsum("qscd,qdf->scf", arrived, w_up, preferred_element_type=jnp.float32)
    else:
        gate_acts = jnp.einsum("scd,df->scf", arrived, w_gate, preferred_element_type=jnp.float32)
        up_acts = jnp.einsum("scd,df->scf", arrived, w_up, preferred_element_type=jnp.float32)
    hidden_acts = (jax.nn.silu(gate_acts) * up_acts).astype(jnp.bfloat16)
    partial_value = jnp.einsum("scf,fd->scd", hidden_acts, w_down, preferred_element_type=jnp.float32)
    return partial_value.astype(jnp.bfloat16)


def body(tokens, w_gate, w_up, w_down, routes, gate_levels, ancestors):
    local_rows = routes.shape[0]
    choose = routes.shape[1]
    groups = lax.axis_size("expert")
    local_experts = w_gate.shape[0]
    experts = local_experts * groups
    capacity = 3 * local_rows * choose // (2 * experts)
    pairs = local_rows * choose
    chosen = routes.reshape(-1)
    one_hot = (chosen[:, None] == jnp.arange(experts, dtype=jnp.int32)[None, :]).astype(jnp.bfloat16)
    lower = jnp.arange(pairs, dtype=jnp.int32)
    tri = (lower[:, None] > lower[None, :]).astype(jnp.bfloat16)
    earlier = jnp.dot(tri, one_hot, preferred_element_type=jnp.float32)
    places = jnp.sum(earlier * one_hot.astype(jnp.float32), 1).astype(jnp.int32)
    target = chosen * capacity + places
    row_ids = jnp.arange(pairs, dtype=jnp.int32) // choose
    picks = (target[:, None] == jnp.arange(experts * capacity, dtype=jnp.int32)[None, :]).astype(jnp.bfloat16)
    slot_rows = jnp.dot(row_ids.astype(jnp.bfloat16), picks, preferred_element_type=jnp.float32).astype(jnp.int32)
    slot_rows = slot_rows.reshape(groups, local_experts, capacity)
    arrived = lax.all_to_all(tokens[slot_rows[:, 0]], "expert", split_axis=0, concat_axis=0, tiled=True)
    full0 = lax.all_gather(arrived, "hidden", axis=0, tiled=False)
    whole_rows = lax.all_gather(tokens, "hidden", axis=1, tiled=True)
    lead = 2 * capacity // 3
    head = lax.all_to_all(whole_rows[slot_rows[:, 1, :lead]], "expert", split_axis=0, concat_axis=0, tiled=True)
    full0, head = lax.optimization_barrier((full0, head))
    part0 = expert_part(full0, w_gate[0], w_up[0], w_down[0])
    summed0 = lax.psum_scatter(part0, "hidden", scatter_dimension=2, tiled=True)
    tail_rows, part0 = lax.optimization_barrier((slot_rows[:, 1, lead:], part0))
    tail = lax.all_to_all(whole_rows[tail_rows], "expert", split_axis=0, concat_axis=0, tiled=True)
    part1 = expert_part(jnp.concatenate([head, tail], 1), w_gate[1], w_up[1], w_down[1])
    summed1 = lax.psum_scatter(part1, "hidden", scatter_dimension=2, tiled=True)
    per_expert = [lax.all_to_all(s, "expert", split_axis=0, concat_axis=0, tiled=True) for s in (summed0, summed1)]
    source = target.reshape(local_rows, choose)[ancestors]
    levels = gate_levels.astype(jnp.float32)[ancestors]
    weights = levels / jnp.sum(levels, 1, keepdims=True)
    slots = jnp.arange(experts * capacity, dtype=jnp.int32)
    mixing = jnp.sum(jnp.where(source[:, :, None] == slots[None, None, :], weights[:, :, None], 0.0), 1)
    mixing = mixing.reshape(local_rows, groups, local_experts, capacity)
    combined = sum(
        jnp.dot(
            mixing[:, :, c].reshape(local_rows, groups * capacity),
            back.reshape(groups * capacity, back.shape[2]).astype(jnp.float32),
            precision=lax.Precision.HIGHEST,
        )
        for c, back in enumerate(per_expert)
    )
    return combined.astype(jnp.bfloat16)


def solution(mesh):
    placed = (
        P("expert", "hidden"),
        P("expert", None, "hidden"),
        P("expert", None, "hidden"),
        P("expert", "hidden", None),
        P("expert", None),
        P("expert", None),
        P("expert"),
    )
    return jax.shard_map(
        body, mesh=mesh, in_specs=placed, out_specs=P("expert", "hidden"), check_vma=False
    )
```

```python
import jax
import jax.numpy as jnp
from jax import lax
from jax.sharding import PartitionSpec as P

def expert_part(arrived, w_gate, w_up, w_down):
    gate_acts = jnp.einsum("scd,df->scf", arrived, w_gate, preferred_element_type=jnp.float32)
    up_acts = jnp.einsum("scd,df->scf", arrived, w_up, preferred_element_type=jnp.float32)
    hidden_acts = lax.optimization_barrier((jax.nn.silu(gate_acts) * up_acts).astype(jnp.bfloat16))
    partial_value = jnp.einsum("scf,fd->scd", hidden_acts, w_down, preferred_element_type=jnp.float32)
    return partial_value.astype(jnp.bfloat16)


def body(tokens, w_gate, w_up, w_down, routes, gate_levels, ancestors):
    local_rows = routes.shape[0]
    choose = routes.shape[1]
    groups = lax.axis_size("expert")
    local_experts = w_gate.shape[0]
    experts = local_experts * groups
    capacity = 3 * local_rows * choose // (2 * experts)
    pairs = local_rows * choose
    chosen = routes.reshape(-1)
    one_hot = (chosen[:, None] == jnp.arange(experts, dtype=jnp.int32)[None, :]).astype(jnp.bfloat16)
    lower = jnp.arange(pairs, dtype=jnp.int32)
    tri = (lower[:, None] > lower[None, :]).astype(jnp.bfloat16)
    earlier = jnp.dot(tri, one_hot, preferred_element_type=jnp.float32)
    places = jnp.sum(earlier * one_hot.astype(jnp.float32), 1).astype(jnp.int32)
    target = chosen * capacity + places
    row_ids = jnp.arange(pairs, dtype=jnp.int32) // choose
    picks = (target[:, None] == jnp.arange(experts * capacity, dtype=jnp.int32)[None, :]).astype(jnp.bfloat16)
    slot_rows = jnp.dot(row_ids.astype(jnp.bfloat16), picks, preferred_element_type=jnp.float32).astype(jnp.int32)
    slot_rows = slot_rows.reshape(groups, local_experts, capacity)
    arrived = lax.all_to_all(tokens[slot_rows[:, 0]], "expert", split_axis=0, concat_axis=0, tiled=True)
    full0 = lax.all_gather(arrived, "hidden", axis=2, tiled=True)
    whole_rows = lax.all_gather(tokens, "hidden", axis=1, tiled=True)
    lead = 2 * capacity // 3
    head = lax.all_to_all(whole_rows[slot_rows[:, 1, :lead]], "expert", split_axis=0, concat_axis=0, tiled=True)
    full0, head = lax.optimization_barrier((full0, head))
    part0 = expert_part(full0, w_gate[0], w_up[0], w_down[0])
    summed0 = lax.psum_scatter(part0, "hidden", scatter_dimension=2, tiled=True)
    tail_rows, part0 = lax.optimization_barrier((slot_rows[:, 1, lead:], part0))
    tail = lax.all_to_all(whole_rows[tail_rows], "expert", split_axis=0, concat_axis=0, tiled=True)
    part1 = expert_part(jnp.concatenate([head, tail], 1), w_gate[1], w_up[1], w_down[1])
    summed1 = lax.psum_scatter(part1, "hidden", scatter_dimension=2, tiled=True)
    per_expert = [lax.all_to_all(s, "expert", split_axis=0, concat_axis=0, tiled=True) for s in (summed0, summed1)]
    source = target.reshape(local_rows, choose)[ancestors]
    levels = gate_levels.astype(jnp.float32)[ancestors]
    weights = levels / jnp.sum(levels, 1, keepdims=True)
    slots = jnp.arange(experts * capacity, dtype=jnp.int32)
    mixing = jnp.sum(jnp.where(source[:, :, None] == slots[None, None, :], weights[:, :, None], 0.0), 1)
    mixing = mixing.reshape(local_rows, groups, local_experts, capacity)
    combined = sum(
        jnp.dot(
            mixing[:, :, c].reshape(local_rows, groups * capacity),
            back.reshape(groups * capacity, back.shape[2]).astype(jnp.float32),
            precision=lax.Precision.HIGHEST,
        )
        for c, back in enumerate(per_expert)
    )
    return combined.astype(jnp.bfloat16)


def solution(mesh):
    placed = (
        P("expert", "hidden"),
        P("expert", None, "hidden"),
        P("expert", None, "hidden"),
        P("expert", "hidden", None),
        P("expert", None),
        P("expert", None),
        P("expert"),
    )
    return jax.shard_map(
        body, mesh=mesh, in_specs=placed, out_specs=P("expert", "hidden"), check_vma=False
    )
```

```python
import jax
import jax.numpy as jnp
from jax import lax
from jax.sharding import PartitionSpec as P

def expert_part(arrived, w_gate, w_up, w_down):
    gate_acts = jnp.einsum("scd,df->scf", arrived, w_gate, preferred_element_type=jnp.float32)
    up_acts = jnp.einsum("scd,df->scf", arrived, w_up, preferred_element_type=jnp.float32)
    hidden_acts = lax.optimization_barrier((jax.nn.silu(gate_acts) * up_acts).astype(jnp.bfloat16))
    partial_value = jnp.einsum("scf,fd->scd", hidden_acts, w_down, preferred_element_type=jnp.float32)
    return partial_value.astype(jnp.bfloat16)


def body(tokens, w_gate, w_up, w_down, routes, gate_levels, ancestors):
    local_rows = routes.shape[0]
    choose = routes.shape[1]
    groups = lax.axis_size("expert")
    local_experts = w_gate.shape[0]
    experts = local_experts * groups
    capacity = 3 * local_rows * choose // (2 * experts)
    pairs = local_rows * choose
    chosen = routes.reshape(-1)
    one_hot = (chosen[:, None] == jnp.arange(experts, dtype=jnp.int32)[None, :]).astype(jnp.bfloat16)
    lower = jnp.arange(pairs, dtype=jnp.int32)
    tri = (lower[:, None] > lower[None, :]).astype(jnp.bfloat16)
    earlier = jnp.dot(tri, one_hot, preferred_element_type=jnp.float32)
    places = jnp.sum(earlier * one_hot.astype(jnp.float32), 1).astype(jnp.int32)
    target = chosen * capacity + places
    row_ids = jnp.arange(pairs, dtype=jnp.int32) // choose
    picks = (target[:, None] == jnp.arange(experts * capacity, dtype=jnp.int32)[None, :]).astype(jnp.bfloat16)
    slot_rows = jnp.dot(row_ids.astype(jnp.bfloat16), picks, preferred_element_type=jnp.float32).astype(jnp.int32)
    slot_rows = slot_rows.reshape(groups, local_experts, capacity)
    arrived = lax.all_to_all(tokens[slot_rows[:, 0]], "expert", split_axis=0, concat_axis=0, tiled=True)
    full0 = lax.all_gather(arrived, "hidden", axis=2, tiled=True)
    whole_rows = lax.all_gather(tokens, "hidden", axis=1, tiled=True)
    lead = 3 * capacity // 4
    head = lax.all_to_all(whole_rows[slot_rows[:, 1, :lead]], "expert", split_axis=0, concat_axis=0, tiled=True)
    full0, head = lax.optimization_barrier((full0, head))
    part0 = expert_part(full0, w_gate[0], w_up[0], w_down[0])
    summed0 = lax.psum_scatter(part0, "hidden", scatter_dimension=2, tiled=True)
    tail_rows, part0 = lax.optimization_barrier((slot_rows[:, 1, lead:], part0))
    tail = lax.all_to_all(whole_rows[tail_rows], "expert", split_axis=0, concat_axis=0, tiled=True)
    part1 = expert_part(jnp.concatenate([head, tail], 1), w_gate[1], w_up[1], w_down[1])
    summed1 = lax.psum_scatter(part1, "hidden", scatter_dimension=2, tiled=True)
    per_expert = [lax.all_to_all(s, "expert", split_axis=0, concat_axis=0, tiled=True) for s in (summed0, summed1)]
    source = target.reshape(local_rows, choose)[ancestors]
    levels = gate_levels.astype(jnp.float32)[ancestors]
    weights = levels / jnp.sum(levels, 1, keepdims=True)
    slots = jnp.arange(experts * capacity, dtype=jnp.int32)
    mixing = jnp.sum(jnp.where(source[:, :, None] == slots[None, None, :], weights[:, :, None], 0.0), 1)
    mixing = mixing.reshape(local_rows, groups, local_experts, capacity)
    combined = sum(
        jnp.dot(
            mixing[:, :, c].reshape(local_rows, groups * capacity),
            back.reshape(groups * capacity, back.shape[2]).astype(jnp.float32),
            precision=lax.Precision.HIGHEST,
        )
        for c, back in enumerate(per_expert)
    )
    return combined.astype(jnp.bfloat16)


def solution(mesh):
    placed = (
        P("expert", "hidden"),
        P("expert", None, "hidden"),
        P("expert", None, "hidden"),
        P("expert", "hidden", None),
        P("expert", None),
        P("expert", None),
        P("expert"),
    )
    return jax.shard_map(
        body, mesh=mesh, in_specs=placed, out_specs=P("expert", "hidden"), check_vma=False
    )
```
